256 devices in a mesh: pipe: 16 (over y, z_hi, core), expert: 16 (over z_lo, x).
Axes of the slice: x: 4, y: 4, z: 8 (z_hi: 2, z_lo: 4; z = z_hi * 4 + z_lo), core: 2. Of those that a mesh axis runs over, the one named last changes fastest.
Arguments:
- tokens_a: bfloat16 [16, 2048, 2048], P('pipe', 'expert'), may hold values from -6 to 6
- cotangent_a: bfloat16 [16, 2048, 2048], P('pipe', 'expert'), may hold values from -6 to 6
- tokens_b: bfloat16 [16, 2048, 2048], P('pipe', 'expert'), may hold values from -6 to 6
- routes_a: int32 [16, 2048, 2], P('pipe', 'expert'), may hold values from 0 to 15, as said below
- routes_b: int32 [16, 2048, 2], P('pipe', 'expert'), may hold values from 0 to 15, as said below
- probs_a: float32 [16, 2048, 2], P('pipe', 'expert'), may hold values from 0.1 to 0.9
- probs_b: float32 [16, 2048, 2], P('pipe', 'expert'), may hold values from 0.1 to 0.9
- w_gate: bfloat16 [16, 16, 2048, 768], P('pipe', 'expert'), may hold values from -0.125 to 0.125
- w_up: bfloat16 [16, 16, 2048, 768], P('pipe', 'expert'), may hold values from -0.125 to 0.125
- w_down: bfloat16 [16, 16, 768, 2048], P('pipe', 'expert'), may hold values from -0.21875 to 0.21875
Outputs:
- grad_a: bfloat16 [16, 2048, 2048], P('pipe', 'expert')
- grad_b: bfloat16 [16, 2048, 2048], P('pipe', 'expert')
The draws below stay inside these ranges and needn't reach their ends.
Inputs may be any that keep to these rules, and one draw needn't show every extreme that they name: `routes_a`: in every section one expert, drawn per section, is named exactly 28 times by the 128 tokens of every aligned block of 128 tokens; no block names any expert more than 28 times; the two experts of a token differ. `routes_b`: in every section one expert, drawn per section, is named exactly 28 times by the 128 tokens of every aligned block of 128 tokens; no block names any expert more than 28 times; the two experts of a token differ.
All inputs are finite; a program needn't handle non-finite values.
Results may differ from the reference program's by a relative error of at most 0.0062.
Values may be sent and summed in bfloat16 or wider, within the bound.
No kernel may reach another device: no remote copies, remote signals or barrier semaphores. Data moves between devices by JAX's collectives and lax.ppermute only.
A program may use at most 64 MiB of HBM per device.

```python
import jax
import jax.numpy as jnp
from jax import lax

D = 2048
FF = 768
TOK_DEV = 128
SECTIONS = 16
EXPERTS = 16
TOKENS = 2048
CAP = 28


def draw_block(key, hot_expert):
    sub_keys = jax.random.split(key, 4)
    expert_order = jax.random.permutation(sub_keys[0], EXPERTS).astype(jnp.int32)
    hot_last = jnp.argsort((expert_order == hot_expert).astype(jnp.int32), stable=True)
    others = expert_order[hot_last][:EXPERTS - 1]
    spare_slots = 2 * TOK_DEV - CAP
    base_count = spare_slots // (EXPERTS - 1)
    extra_count = spare_slots % (EXPERTS - 1)
    reach_max = min(base_count, CAP - base_count - 1)
    swing_size = jax.random.randint(sub_keys[1], ((EXPERTS - 1) // 2,), 0, reach_max + 1).astype(jnp.int32)
    signed = jnp.stack([swing_size, -swing_size], axis=1).reshape(-1)
    if (EXPERTS - 1) % 2 == 1:
        signed = jnp.concatenate([signed, jnp.zeros((1,), jnp.int32)])
    counts = base_count + (jnp.arange(EXPERTS - 1, dtype=jnp.int32) < extra_count).astype(jnp.int32) + signed
    count_ends = jnp.cumsum(counts)
    labels = jnp.sum((jnp.arange(spare_slots, dtype=jnp.int32)[:, None] >= count_ends[None, :]).astype(jnp.int32), axis=1)
    chosen = others[labels]
    pair_count = TOK_DEV - CAP
    first_col = chosen[:pair_count]
    second = chosen[pair_count:2 * pair_count]
    single = chosen[2 * pair_count:]
    column_zero = jnp.concatenate([jnp.full((CAP,), hot_expert, jnp.int32), first_col])
    column_one = jnp.concatenate([single, second])
    position = jax.random.permutation(sub_keys[2], TOK_DEV)
    left_side = column_zero[position]
    right_side = column_one[position]
    flip_bits = jax.random.randint(sub_keys[3], (TOK_DEV,), 0, 2)
    route_one = jnp.where(flip_bits == 1, right_side, left_side)
    route_two = jnp.where(flip_bits == 1, left_side, right_side)
    return jnp.stack([route_one, route_two], axis=1).astype(jnp.int32)


def section_rows(key):
    sub_keys = jax.random.split(key, EXPERTS + 1)
    hot_expert = jax.random.randint(sub_keys[0], (), 0, EXPERTS).astype(jnp.int32)
    blocks = jax.vmap(lambda block_key: draw_block(block_key, hot_expert))(sub_keys[1:])
    return blocks.reshape(TOKENS, 2)


def draw_routes_a(key, part):
    base_key = jax.random.fold_in(key, 11)
    return jax.vmap(section_rows)(jax.random.split(base_key, SECTIONS))


def draw_routes_b(key, part):
    base_key = jax.random.fold_in(key, 23)
    return jax.vmap(section_rows)(jax.random.split(base_key, SECTIONS))


def steps_of(own_key, dims, cuts, smallest, top_value):
    gain, own = 1.0, jax.random.fold_in(own_key, 6)
    for dim, parts in cuts:
        draws = jnp.exp(jax.random.uniform(jax.random.fold_in(own, dim), (parts,), jnp.float32, smallest / len(cuts), top_value / len(cuts)))
        gain = gain * jnp.repeat(draws, dims[dim] // parts).reshape([-1 if axis == dim else 1 for axis in range(len(dims))])
    return gain


def bell_draw(rng, shape, spread, most, cuts=(), kind=jnp.bfloat16):
    factor_of = steps_of(rng, shape, cuts, -0.22, 0.18) if cuts else 1.0
    values = jax.random.normal(rng, shape, jnp.float32) * spread * factor_of
    return jnp.minimum(jnp.maximum(values, -most), most).astype(kind)


def setup_inputs(seed: int = 0) -> dict:
    splits = jax.random.split(jax.random.key(seed), 11)
    tokens_a = bell_draw(splits[0], (SECTIONS, TOKENS, D), 1.0, 6.0, ((0, 16), (1, 16)))
    cotangent_a = bell_draw(splits[1], (SECTIONS, TOKENS, D), 1.0, 6.0, ((0, 16), (1, 16)))
    tokens_b = bell_draw(splits[2], (SECTIONS, TOKENS, D), 1.0, 6.0, ((0, 16), (1, 16)))
    routes_a = draw_routes_a(jax.random.fold_in(splits[10], 71), 0)
    routes_b = draw_routes_b(jax.random.fold_in(splits[10], 71), 0)
    probs_a = jnp.clip(0.1 + 0.79999997 * jax.random.uniform(splits[5], (SECTIONS, TOKENS, 2), jnp.float32) ** steps_of(splits[5], (SECTIONS, TOKENS, 2), ((0, 16), (1, 16)), -0.2, 0.2), 0.1, 0.9)
    probs_b = jnp.clip(0.1 + 0.79999997 * jax.random.uniform(splits[6], (SECTIONS, TOKENS, 2), jnp.float32) ** steps_of(splits[6], (SECTIONS, TOKENS, 2), ((0, 16), (1, 16)), -0.2, 0.2), 0.1, 0.9)
    w_gate = bell_draw(splits[7], (SECTIONS, EXPERTS, D, FF), D ** -0.5, 0.125, ((0, 16), (1, 16)))
    w_up = bell_draw(splits[8], (SECTIONS, EXPERTS, D, FF), D ** -0.5, 0.125, ((0, 16), (1, 16)))
    w_down = bell_draw(splits[9], (SECTIONS, EXPERTS, FF, D), FF ** -0.5, 0.21875, ((0, 16), (1, 16)))
    return dict(tokens_a=tokens_a, cotangent_a=cotangent_a, tokens_b=tokens_b, routes_a=routes_a, routes_b=routes_b, probs_a=probs_a, probs_b=probs_b, w_gate=w_gate, w_up=w_up, w_down=w_down)


def slot_table(routes, experts):
    route_hits = (routes[:, :, None] == jnp.arange(experts, dtype=jnp.int32)[None, None, :]).astype(jnp.int32)
    per_token = lax.optimization_barrier(jnp.sum(route_hits, axis=1))
    before = jnp.cumsum(per_token, axis=0) - per_token
    return lax.optimization_barrier(jnp.sum(route_hits * before[:, None, :], axis=2)).astype(jnp.int32)

def token_rows(tokens):
    return jnp.broadcast_to(tokens[:, None, :], (tokens.shape[0], 2, tokens.shape[1]))

def scaled_rows(cotangent, probs):
    return (probs[:, :, None] * cotangent[:, None, :].astype(jnp.float32)).astype(jnp.bfloat16)

def recompute(flat_rows, gate_mat, up_mat):
    gate_pre = jnp.dot(flat_rows, gate_mat, preferred_element_type=jnp.float32)
    up_pre = jnp.dot(flat_rows, up_mat, preferred_element_type=jnp.float32)
    return (gate_pre, up_pre)

def backprop(gate_pre, up_pre, flat_scaled, gate_mat, up_mat, down_mat):
    contract = (((1,), (1,)), ((), ()))
    d_hidden = lax.dot_general(flat_scaled, down_mat, contract, preferred_element_type=jnp.float32)
    gate_sig = jax.nn.sigmoid(gate_pre)
    active = gate_pre * gate_sig
    slope = gate_sig * (1.0 + gate_pre * (1.0 - gate_sig))
    d_gate = (d_hidden * up_pre * slope).astype(jnp.bfloat16)
    d_up = (d_hidden * active).astype(jnp.bfloat16)
    back = lax.dot_general(d_gate, gate_mat, contract, preferred_element_type=jnp.float32)
    back = back + lax.dot_general(d_up, up_mat, contract, preferred_element_type=jnp.float32)
    return back.astype(jnp.bfloat16)

def block_grad(tokens, cotangent, routes, probs, gate_all, up_all, down_all):
    experts = gate_all.shape[0]
    tok_count = tokens.shape[0] // experts
    width = tokens.shape[1]
    capacity = 7 * tok_count // (2 * experts)
    block_routes = routes.reshape(experts, tok_count, 2)
    slot_index = jax.vmap(lambda single: slot_table(single, experts))(block_routes)
    source_ids = jnp.broadcast_to(jnp.arange(experts, dtype=jnp.int32)[:, None, None], block_routes.shape)
    rows_tokens = token_rows(tokens).reshape(experts, tok_count, 2, width)
    rows_scaled = scaled_rows(cotangent, probs).reshape(experts, tok_count, 2, width)
    empty = jnp.zeros((experts, experts, capacity, width), jnp.bfloat16)
    buffer_tokens = empty.at[block_routes, source_ids, slot_index].set(rows_tokens)
    buffer_scaled = empty.at[block_routes, source_ids, slot_index].set(rows_scaled)

    def per_expert(pieces):
        held_tokens, held_scaled, gate_mat, up_mat, down_mat = pieces
        gate_pre, up_pre = recompute(held_tokens.reshape(-1, width), gate_mat, up_mat)
        grad_rows = backprop(gate_pre, up_pre, held_scaled.reshape(-1, width), gate_mat, up_mat, down_mat)
        return grad_rows.reshape(experts, capacity, width)
    results = lax.map(per_expert, (buffer_tokens, buffer_scaled, gate_all, up_all, down_all))
    picked = results[block_routes, source_ids, slot_index]
    summed = cotangent.astype(jnp.float32) + lax.optimization_barrier(jnp.sum(picked.astype(jnp.float32), axis=2)).reshape(-1, width)
    return summed.astype(jnp.bfloat16)

def reference(tokens_a, cotangent_a, tokens_b, routes_a, routes_b, probs_a, probs_b, w_gate, w_up, w_down):
    grad_a = lax.map(lambda pieces: block_grad(*pieces), (tokens_a, cotangent_a, routes_a, probs_a, w_gate, w_up, w_down))
    second_cot = jnp.roll(grad_a, -1, axis=0)
    grad_b = lax.map(lambda pieces: block_grad(*pieces), (tokens_b, second_cot, routes_b, probs_b, w_gate, w_up, w_down))
    return (grad_a, grad_b)
```

```python
import jax
import jax.numpy as jnp
from jax import lax
from jax.sharding import PartitionSpec as P


def shifted(block, axis, distance):
    devices = range(lax.axis_size(axis))
    route = [((i - distance) % len(devices), i) for i in devices]
    return lax.ppermute(block, axis, route)


def slot_table(routes, experts):
    route_hits = (routes[:, :, None] == jnp.arange(experts, dtype=jnp.int32)[None, None, :]).astype(
        jnp.int32
    )
    per_token = jnp.sum(route_hits, axis=1)
    before = jnp.cumsum(per_token, axis=0) - per_token
    return jnp.sum(route_hits * before[:, None, :], axis=2)


def slot_hits(routes, experts, capacity):
    slot_index = slot_table(routes, experts)
    flat_ids = routes * capacity + slot_index
    targets = jnp.arange(experts * capacity, dtype=jnp.int32)
    hits = (flat_ids[:, :, None] == targets[None, None, :]).astype(jnp.bfloat16)
    return hits.reshape(routes.shape[0], 2, experts, capacity)


def place_tokens(tokens, hits):
    table = jnp.sum(hits, axis=1)
    packed = lax.dot_general(
        table, tokens, (((0,), (0,)), ((), ())), preferred_element_type=jnp.float32
    )
    return packed.astype(jnp.bfloat16)


def place_scaled(cotangent, probs, hits):
    rows = (probs[:, :, None] * cotangent[:, None, :].astype(jnp.float32)).astype(jnp.bfloat16)
    packed = lax.dot_general(
        hits, rows, (((0, 1), (0, 1)), ((), ())), preferred_element_type=jnp.float32
    )
    return packed.astype(jnp.bfloat16)


def recompute(rows, gate_mat, up_mat):
    contract = (((2,), (0,)), ((), ()))
    gate_pre = lax.dot_general(rows, gate_mat, contract, preferred_element_type=jnp.float32)
    up_pre = lax.dot_general(rows, up_mat, contract, preferred_element_type=jnp.float32)
    return (gate_pre, up_pre)


def backprop(gate_pre, up_pre, scaled, gate_mat, up_mat, down_mat):
    contract = (((2,), (1,)), ((), ()))
    d_hidden = lax.dot_general(scaled, down_mat, contract, preferred_element_type=jnp.float32)
    gate_sig = jax.nn.sigmoid(gate_pre)
    active = gate_pre * gate_sig
    slope = gate_sig * (1.0 + gate_pre * (1.0 - gate_sig))
    d_gate = (d_hidden * up_pre * slope).astype(jnp.bfloat16)
    d_up = (d_hidden * active).astype(jnp.bfloat16)
    back = lax.dot_general(d_gate, gate_mat, contract, preferred_element_type=jnp.float32)
    back = back + lax.dot_general(d_up, up_mat, contract, preferred_element_type=jnp.float32)
    return back.astype(jnp.bfloat16)


def send_out(blocks):
    n = blocks.shape[0]
    out = [blocks[0]]
    for k in range(1, n):
        out.append(lax.ppermute(blocks[k], "expert", [(i, (i + k) % n) for i in range(n)]))
    return out


def send_home(blocks):
    n = len(blocks)
    out = [blocks[0]]
    for k in range(1, n):
        out.append(lax.ppermute(blocks[k], "expert", [((i + k) % n, i) for i in range(n)]))
    return jnp.stack(out)


def pick(returned, hits, cotangent):
    table = jnp.sum(hits, axis=1)
    picked = lax.dot_general(
        table, returned, (((1, 2), (0, 1)), ((), ())), preferred_element_type=jnp.float32
    )
    summed = cotangent.astype(jnp.float32) + picked
    return summed.astype(jnp.bfloat16)


GROUPS = 2


def grouped(blocks):
    size = len(blocks) // GROUPS
    return [jnp.stack(blocks[g * size:(g + 1) * size]) for g in range(GROUPS)]


def ungrouped(groups):
    return [g[i] for g in groups for i in range(g.shape[0])]


def on_device(
    tokens_a, cotangent_a, tokens_b, routes_a, routes_b, probs_a, probs_b, w_gate, w_up, w_down
):
    experts = lax.axis_size("expert")
    me = lax.axis_index("expert")
    tok_count = tokens_a.shape[1]
    capacity = 7 * tok_count // (2 * experts)
    gate_mat = w_gate[0, 0]
    up_mat = w_up[0, 0]
    down_mat = w_down[0, 0]
    first_hits = slot_hits((routes_a[0] - me) % experts, experts, capacity)
    second_hits = slot_hits((routes_b[0] - me) % experts, experts, capacity)
    first_cot = cotangent_a[0]

    first_tokens = grouped(send_out(place_tokens(tokens_a[0], first_hits)))
    first_scaled = grouped(send_out(place_scaled(first_cot, probs_a[0], first_hits)))
    second_packed = place_tokens(tokens_b[0], second_hits)
    first_tokens, first_scaled, second_packed = lax.optimization_barrier(
        (first_tokens, first_scaled, second_packed)
    )
    second_tokens = grouped(send_out(second_packed))

    first_rows = []
    for held_tokens, held_scaled in zip(first_tokens, first_scaled):
        gate_pre, up_pre = recompute(held_tokens, gate_mat, up_mat)
        first_rows.append(backprop(gate_pre, up_pre, held_scaled, gate_mat, up_mat, down_mat))
    grad_a = pick(send_home(ungrouped(first_rows)), first_hits, first_cot)

    second_cot = shifted(grad_a, "pipe", -1)
    second_pre = [recompute(held, gate_mat, up_mat) for held in second_tokens]
    second_scaled = grouped(send_out(place_scaled(second_cot, probs_b[0], second_hits)))
    second_rows = []
    for (gate_pre, up_pre), held_scaled in zip(second_pre, second_scaled):
        second_rows.append(backprop(gate_pre, up_pre, held_scaled, gate_mat, up_mat, down_mat))
    grad_b = pick(send_home(ungrouped(second_rows)), second_hits, second_cot)
    return (grad_a[None], grad_b[None])


def solution(mesh):
    in_specs = (
        P("pipe", "expert", None),
        P("pipe", "expert", None),
        P("pipe", "expert", None),
        P("pipe", "expert", None),
        P("pipe", "expert", None),
        P("pipe", "expert", None),
        P("pipe", "expert", None),
        P("pipe", "expert", None, None),
        P("pipe", "expert", None, None),
        P("pipe", "expert", None, None),
    )
    out_specs = (P("pipe", "expert", None), P("pipe", "expert", None))
    return jax.shard_map(
        on_device, mesh=mesh, in_specs=in_specs, out_specs=out_specs, check_vma=False
    )
```

```python
import jax
import jax.numpy as jnp
from jax import lax
from jax.sharding import PartitionSpec as P


def shifted(block, axis, distance):
    devices = range(lax.axis_size(axis))
    route = [((i - distance) % len(devices), i) for i in devices]
    return lax.ppermute(block, axis, route)


def slot_table(routes, experts):
    route_hits = (routes[:, :, None] == jnp.arange(experts, dtype=jnp.int32)[None, None, :]).astype(
        jnp.int32
    )
    per_token = jnp.sum(route_hits, axis=1)
    before = jnp.cumsum(per_token, axis=0) - per_token
    return jnp.sum(route_hits * before[:, None, :], axis=2)


def slot_hits(routes, experts, capacity):
    slot_index = slot_table(routes, experts)
    flat_ids = routes * capacity + slot_index
    targets = jnp.arange(experts * capacity, dtype=jnp.int32)
    hits = (flat_ids[:, :, None] == targets[None, None, :]).astype(jnp.bfloat16)
    return hits.reshape(routes.shape[0], 2, experts, capacity)


def scaled_rows(cotangent, probs):
    return (probs[:, :, None] * cotangent[:, None, :].astype(jnp.float32)).astype(jnp.bfloat16)


def place(hits, rows):
    packed = lax.dot_general(
        hits, rows, (((0, 1), (0, 1)), ((), ())), preferred_element_type=jnp.float32
    )
    return packed.astype(jnp.bfloat16)


def place_tokens(tokens, hits):
    table = jnp.sum(hits, axis=1)
    packed = lax.dot_general(
        table, tokens, (((0,), (0,)), ((), ())), preferred_element_type=jnp.float32
    )
    return packed.astype(jnp.bfloat16)


def recompute(rows, gate_mat, up_mat):
    contract = (((2,), (0,)), ((), ()))
    gate_pre = lax.dot_general(rows, gate_mat, contract, preferred_element_type=jnp.float32)
    up_pre = lax.dot_general(rows, up_mat, contract, preferred_element_type=jnp.float32)
    return (gate_pre, up_pre)


def backprop(gate_pre, up_pre, scaled, gate_mat, up_mat, down_mat):
    contract = (((2,), (1,)), ((), ()))
    d_hidden = lax.dot_general(scaled, down_mat, contract, preferred_element_type=jnp.float32)
    gate_sig = jax.nn.sigmoid(gate_pre)
    active = gate_pre * gate_sig
    slope = gate_sig * (1.0 + gate_pre * (1.0 - gate_sig))
    d_gate = (d_hidden * up_pre * slope).astype(jnp.bfloat16)
    d_up = (d_hidden * active).astype(jnp.bfloat16)
    back = lax.dot_general(d_gate, gate_mat, contract, preferred_element_type=jnp.float32)
    back = back + lax.dot_general(d_up, up_mat, contract, preferred_element_type=jnp.float32)
    return back.astype(jnp.bfloat16)


def exchange(block):
    return lax.all_to_all(block, "expert", split_axis=0, concat_axis=0, tiled=True)


def pick(returned, hits, cotangent):
    table = jnp.sum(hits, axis=1)
    picked = lax.dot_general(
        table, returned, (((1, 2), (0, 1)), ((), ())), preferred_element_type=jnp.float32
    )
    summed = cotangent.astype(jnp.float32) + picked
    return summed.astype(jnp.bfloat16)


def on_device(
    tokens_a, cotangent_a, tokens_b, routes_a, routes_b, probs_a, probs_b, w_gate, w_up, w_down
):
    experts = lax.axis_size("expert")
    tok_count = tokens_a.shape[1]
    width = tokens_a.shape[2]
    capacity = 7 * tok_count // (2 * experts)
    gate_mat = w_gate[0, 0]
    up_mat = w_up[0, 0]
    down_mat = w_down[0, 0]
    first_hits = slot_hits(routes_a[0], experts, capacity)
    second_hits = slot_hits(routes_b[0], experts, capacity)
    first_cot = cotangent_a[0]

    first_rows = jnp.concatenate(
        [
            jnp.broadcast_to(tokens_a[0][:, None, :], (tok_count, 2, width)),
            scaled_rows(first_cot, probs_a[0]),
        ],
        axis=2,
    )
    first_arrived = exchange(place(first_hits, first_rows))
    gate_pre, up_pre = recompute(first_arrived[:, :, :width], gate_mat, up_mat)
    first_back = backprop(
        gate_pre, up_pre, first_arrived[:, :, width:], gate_mat, up_mat, down_mat
    )
    second_tokens = place_tokens(tokens_b[0], second_hits)
    mixed = exchange(jnp.concatenate([first_back, second_tokens], axis=2))
    grad_a = pick(mixed[:, :, :width], first_hits, first_cot)

    second_cot = shifted(grad_a, "pipe", -1)
    second_gate_pre, second_up_pre = recompute(mixed[:, :, width:], gate_mat, up_mat)
    second_scaled = exchange(place(second_hits, scaled_rows(second_cot, probs_b[0])))
    second_back = backprop(
        second_gate_pre, second_up_pre, second_scaled, gate_mat, up_mat, down_mat
    )
    grad_b = pick(exchange(second_back), second_hits, second_cot)
    return (grad_a[None], grad_b[None])


def solution(mesh):
    in_specs = (
        P("pipe", "expert", None),
        P("pipe", "expert", None),
        P("pipe", "expert", None),
        P("pipe", "expert", None),
        P("pipe", "expert", None),
        P("pipe", "expert", None),
        P("pipe", "expert", None),
        P("pipe", "expert", None, None),
        P("pipe", "expert", None, None),
        P("pipe", "expert", None, None),
    )
    out_specs = (P("pipe", "expert", None), P("pipe", "expert", None))
    return jax.shard_map(
        on_device, mesh=mesh, in_specs=in_specs, out_specs=out_specs, check_vma=False
    )
```

```python
import jax
import jax.numpy as jnp
from jax import lax
from jax.sharding import PartitionSpec as P


def shifted(block, axis, distance):
    devices = range(lax.axis_size(axis))
    route = [((i - distance) % len(devices), i) for i in devices]
    return lax.ppermute(block, axis, route)


def slot_table(routes, experts):
    route_hits = (routes[:, :, None] == jnp.arange(experts, dtype=jnp.int32)[None, None, :]).astype(
        jnp.int32
    )
    per_token = jnp.sum(route_hits, axis=1)
    before = jnp.cumsum(per_token, axis=0) - per_token
    return jnp.sum(route_hits * before[:, None, :], axis=2)


def slot_hits(routes, experts, capacity):
    slot_index = slot_table(routes, experts)
    flat_ids = routes * capacity + slot_index
    targets = jnp.arange(experts * capacity, dtype=jnp.int32)
    hits = (flat_ids[:, :, None] == targets[None, None, :]).astype(jnp.bfloat16)
    return hits.reshape(routes.shape[0], 2, experts, capacity)


def scaled_rows(cotangent, probs):
    return (probs[:, :, None] * cotangent[:, None, :].astype(jnp.float32)).astype(jnp.bfloat16)


def place(hits, rows):
    packed = lax.dot_general(
        hits, rows, (((0, 1), (0, 1)), ((), ())), preferred_element_type=jnp.float32
    )
    return packed.astype(jnp.bfloat16)


def place_tokens(tokens, hits):
    table = jnp.sum(hits, axis=1)
    packed = lax.dot_general(
        table, tokens, (((0,), (0,)), ((), ())), preferred_element_type=jnp.float32
    )
    return packed.astype(jnp.bfloat16)


def recompute(rows, gate_mat, up_mat):
    contract = (((2,), (0,)), ((), ()))
    gate_pre = lax.dot_general(rows, gate_mat, contract, preferred_element_type=jnp.float32)
    up_pre = lax.dot_general(rows, up_mat, contract, preferred_element_type=jnp.float32)
    return (gate_pre, up_pre)


def backprop(gate_pre, up_pre, scaled, gate_mat, up_mat, down_mat):
    contract = (((2,), (1,)), ((), ()))
    d_hidden = lax.dot_general(scaled, down_mat, contract, preferred_element_type=jnp.float32)
    gate_sig = jax.nn.sigmoid(gate_pre)
    active = gate_pre * gate_sig
    slope = gate_sig * (1.0 + gate_pre * (1.0 - gate_sig))
    d_gate = (d_hidden * up_pre * slope).astype(jnp.bfloat16)
    d_up = (d_hidden * active).astype(jnp.bfloat16)
    back = lax.dot_general(d_gate, gate_mat, contract, preferred_element_type=jnp.float32)
    back = back + lax.dot_general(d_up, up_mat, contract, preferred_element_type=jnp.float32)
    return back.astype(jnp.bfloat16)


def exchange(block):
    return lax.all_to_all(block, "expert", split_axis=0, concat_axis=0, tiled=True)


def pick(returned, hits, cotangent):
    table = jnp.sum(hits, axis=1)
    picked = lax.dot_general(
        table, returned, (((1, 2), (0, 1)), ((), ())), preferred_element_type=jnp.float32
    )
    summed = cotangent.astype(jnp.float32) + picked
    return summed.astype(jnp.bfloat16)


def back_half(d_gate, d_up, gate_mat, up_mat):
    contract = (((2,), (1,)), ((), ()))
    back = lax.dot_general(d_gate, gate_mat, contract, preferred_element_type=jnp.float32)
    back = back + lax.dot_general(d_up, up_mat, contract, preferred_element_type=jnp.float32)
    return back.astype(jnp.bfloat16)


def hidden_grads(gate_pre, up_pre, scaled, down_mat):
    contract = (((2,), (1,)), ((), ()))
    d_hidden = lax.dot_general(scaled, down_mat, contract, preferred_element_type=jnp.float32)
    gate_sig = jax.nn.sigmoid(gate_pre)
    active = gate_pre * gate_sig
    slope = gate_sig * (1.0 + gate_pre * (1.0 - gate_sig))
    d_gate = (d_hidden * up_pre * slope).astype(jnp.bfloat16)
    d_up = (d_hidden * active).astype(jnp.bfloat16)
    return d_gate, d_up


def pick_cols(returned, table):
    return lax.dot_general(
        table, returned, (((1, 2), (0, 1)), ((), ())), preferred_element_type=jnp.float32
    )


def on_device(
    tokens_a, cotangent_a, tokens_b, routes_a, routes_b, probs_a, probs_b, w_gate, w_up, w_down
):
    experts = lax.axis_size("expert")
    tok_count = tokens_a.shape[1]
    width = tokens_a.shape[2]
    half = width // 2
    capacity = 7 * tok_count // (2 * experts)
    gate_mat = w_gate[0, 0]
    up_mat = w_up[0, 0]
    down_mat = w_down[0, 0]
    first_hits = slot_hits(routes_a[0], experts, capacity)
    second_hits = slot_hits(routes_b[0], experts, capacity)
    first_table = jnp.sum(first_hits, axis=1)
    second_table = jnp.sum(second_hits, axis=1)
    first_cot = cotangent_a[0]

    first_tokens = exchange(place_tokens(tokens_a[0], first_hits))
    first_scaled = exchange(place(first_hits, scaled_rows(first_cot, probs_a[0])))
    gate_pre, up_pre = recompute(first_tokens, gate_mat, up_mat)
    d_gate, d_up = hidden_grads(gate_pre, up_pre, first_scaled, down_mat)
    lead = exchange(back_half(d_gate, d_up, gate_mat[:half], up_mat[:half]))
    second_tokens = place_tokens(tokens_b[0], second_hits)
    mixed = exchange(
        jnp.concatenate([back_half(d_gate, d_up, gate_mat[half:], up_mat[half:]), second_tokens], axis=2)
    )
    picked = jnp.concatenate(
        [pick_cols(lead, first_table), pick_cols(mixed[:, :, :half], first_table)], axis=1
    )
    grad_a = (first_cot.astype(jnp.float32) + picked).astype(jnp.bfloat16)

    second_cot = shifted(grad_a, "pipe", -1)
    gate_pre, up_pre = recompute(mixed[:, :, half:], gate_mat, up_mat)
    second_scaled = exchange(place(second_hits, scaled_rows(second_cot, probs_b[0])))
    d_gate, d_up = hidden_grads(gate_pre, up_pre, second_scaled, down_mat)
    lead = exchange(back_half(d_gate, d_up, gate_mat[:half], up_mat[:half]))
    trail = exchange(back_half(d_gate, d_up, gate_mat[half:], up_mat[half:]))
    picked = jnp.concatenate(
        [pick_cols(lead, second_table), pick_cols(trail, second_table)], axis=1
    )
    grad_b = (second_cot.astype(jnp.float32) + picked).astype(jnp.bfloat16)
    return (grad_a[None], grad_b[None])


def solution(mesh):
    in_specs = (
        P("pipe", "expert", None),
        P("pipe", "expert", None),
        P("pipe", "expert", None),
        P("pipe", "expert", None),
        P("pipe", "expert", None),
        P("pipe", "expert", None),
        P("pipe", "expert", None),
        P("pipe", "expert", None, None),
        P("pipe", "expert", None, None),
        P("pipe", "expert", None, None),
    )
    out_specs = (P("pipe", "expert", None), P("pipe", "expert", None))
    return jax.shard_map(
        on_device, mesh=mesh, in_specs=in_specs, out_specs=out_specs, check_vma=False
    )
```

```python
import jax
import jax.numpy as jnp
from jax import lax
from jax.sharding import PartitionSpec as P


def shifted(block, axis, distance):
    devices = range(lax.axis_size(axis))
    route = [((i - distance) % len(devices), i) for i in devices]
    return lax.ppermute(block, axis, route)


def slot_table(routes, experts):
    route_hits = (routes[:, :, None] == jnp.arange(experts, dtype=jnp.int32)[None, None, :]).astype(
        jnp.int32
    )
    per_token = jnp.sum(route_hits, axis=1)
    before = jnp.cumsum(per_token, axis=0) - per_token
    return jnp.sum(route_hits * before[:, None, :], axis=2)


def slot_hits(routes, experts, capacity):
    slot_index = slot_table(routes, experts)
    flat_ids = routes * capacity + slot_index
    targets = jnp.arange(experts * capacity, dtype=jnp.int32)
    hits = (flat_ids[:, :, None] == targets[None, None, :]).astype(jnp.bfloat16)
    return hits.reshape(routes.shape[0], 2, experts, capacity)


def scaled_rows(cotangent, probs):
    return (probs[:, :, None] * cotangent[:, None, :].astype(jnp.float32)).astype(jnp.bfloat16)


def place(hits, rows):
    packed = lax.dot_general(
        hits, rows, (((0, 1), (0, 1)), ((), ())), preferred_element_type=jnp.float32
    )
    return packed.astype(jnp.bfloat16)


def place_tokens(tokens, hits):
    table = jnp.sum(hits, axis=1)
    packed = lax.dot_general(
        table, tokens, (((0,), (0,)), ((), ())), preferred_element_type=jnp.float32
    )
    return packed.astype(jnp.bfloat16)


def recompute(rows, gate_mat, up_mat):
    contract = (((2,), (0,)), ((), ()))
    gate_pre = lax.dot_general(rows, gate_mat, contract, preferred_element_type=jnp.float32)
    up_pre = lax.dot_general(rows, up_mat, contract, preferred_element_type=jnp.float32)
    return (gate_pre, up_pre)


def backprop(gate_pre, up_pre, scaled, gate_mat, up_mat, down_mat):
    contract = (((2,), (1,)), ((), ()))
    d_hidden = lax.dot_general(scaled, down_mat, contract, preferred_element_type=jnp.float32)
    gate_sig = jax.nn.sigmoid(gate_pre)
    active = gate_pre * gate_sig
    slope = gate_sig * (1.0 + gate_pre * (1.0 - gate_sig))
    d_gate = (d_hidden * up_pre * slope).astype(jnp.bfloat16)
    d_up = (d_hidden * active).astype(jnp.bfloat16)
    back = lax.dot_general(d_gate, gate_mat, contract, preferred_element_type=jnp.float32)
    back = back + lax.dot_general(d_up, up_mat, contract, preferred_element_type=jnp.float32)
    return back.astype(jnp.bfloat16)


def exchange(block):
    return lax.all_to_all(block, "expert", split_axis=0, concat_axis=0, tiled=True)


def pick(returned, hits, cotangent):
    table = jnp.sum(hits, axis=1)
    picked = lax.dot_general(
        table, returned, (((1, 2), (0, 1)), ((), ())), preferred_element_type=jnp.float32
    )
    summed = cotangent.astype(jnp.float32) + picked
    return summed.astype(jnp.bfloat16)


def back_half(d_gate, d_up, gate_mat, up_mat):
    contract = (((2,), (1,)), ((), ()))
    back = lax.dot_general(d_gate, gate_mat, contract, preferred_element_type=jnp.float32)
    back = back + lax.dot_general(d_up, up_mat, contract, preferred_element_type=jnp.float32)
    return back.astype(jnp.bfloat16)


def hidden_grads(gate_pre, up_pre, scaled, down_mat):
    contract = (((2,), (1,)), ((), ()))
    d_hidden = lax.dot_general(scaled, down_mat, contract, preferred_element_type=jnp.float32)
    gate_sig = jax.nn.sigmoid(gate_pre)
    active = gate_pre * gate_sig
    slope = gate_sig * (1.0 + gate_pre * (1.0 - gate_sig))
    d_gate = (d_hidden * up_pre * slope).astype(jnp.bfloat16)
    d_up = (d_hidden * active).astype(jnp.bfloat16)
    return d_gate, d_up


def pick_cols(returned, table):
    return lax.dot_general(
        table, returned, (((1, 2), (0, 1)), ((), ())), preferred_element_type=jnp.float32
    )


def beside(send, filler_input, filler):
    send, filler_input = lax.optimization_barrier((send, filler_input))
    arrived = exchange(send)
    extra = filler(filler_input)
    return lax.optimization_barrier((arrived, extra))


def on_device(
    tokens_a, cotangent_a, tokens_b, routes_a, routes_b, probs_a, probs_b, w_gate, w_up, w_down
):
    experts = lax.axis_size("expert")
    tok_count = tokens_a.shape[1]
    width = tokens_a.shape[2]
    capacity = 7 * tok_count // (2 * experts)
    gate_mat = w_gate[0, 0]
    up_mat = w_up[0, 0]
    down_mat = w_down[0, 0]
    contract = (((2,), (0,)), ((), ()))
    first_hits = slot_hits(routes_a[0], experts, capacity)
    second_hits = slot_hits(routes_b[0], experts, capacity)
    first_cot = cotangent_a[0]

    first_rows = jnp.concatenate(
        [
            jnp.broadcast_to(tokens_a[0][:, None, :], (tok_count, 2, width)),
            scaled_rows(first_cot, probs_a[0]),
            jnp.zeros((tok_count, 2, width), jnp.bfloat16),
        ],
        axis=2,
    )
    first_send = place(first_hits, first_rows)
    second_send = place_tokens(tokens_b[0], second_hits)
    first_send = lax.dynamic_update_slice(first_send, second_send, (0, 0, 2 * width))
    first_arrived, first_table = beside(
        first_send, first_hits, lambda hits: jnp.sum(hits, axis=1)
    )

    gate_pre, up_pre = recompute(first_arrived[:, :, :width], gate_mat, up_mat)
    first_back = backprop(
        gate_pre, up_pre, first_arrived[:, :, width:2 * width], gate_mat, up_mat, down_mat
    )
    second_tokens = first_arrived[:, :, 2 * width:]
    returned, second_gate_pre = beside(
        first_back,
        second_tokens,
        lambda rows: lax.dot_general(rows, gate_mat, contract, preferred_element_type=jnp.float32),
    )
    picked = lax.dot_general(
        first_table, returned, (((1, 2), (0, 1)), ((), ())), preferred_element_type=jnp.float32
    )
    grad_a = (first_cot.astype(jnp.float32) + picked).astype(jnp.bfloat16)

    second_cot = shifted(grad_a, "pipe", -1)
    second_scaled, second_up_pre = beside(
        place(second_hits, scaled_rows(second_cot, probs_b[0])),
        second_tokens,
        lambda rows: lax.dot_general(rows, up_mat, contract, preferred_element_type=jnp.float32),
    )
    second_back = backprop(
        second_gate_pre, second_up_pre, second_scaled, gate_mat, up_mat, down_mat
    )
    second_returned, second_table = beside(
        second_back, second_hits, lambda hits: jnp.sum(hits, axis=1)
    )
    picked = lax.dot_general(
        second_table, second_returned, (((1, 2), (0, 1)), ((), ())),
        preferred_element_type=jnp.float32,
    )
    grad_b = (second_cot.astype(jnp.float32) + picked).astype(jnp.bfloat16)
    return (grad_a[None], grad_b[None])


def solution(mesh):
    in_specs = (
        P("pipe", "expert", None),
        P("pipe", "expert", None),
        P("pipe", "expert", None),
        P("pipe", "expert", None),
        P("pipe", "expert", None),
        P("pipe", "expert", None),
        P("pipe", "expert", None),
        P("pipe", "expert", None, None),
        P("pipe", "expert", None, None),
        P("pipe", "expert", None, None),
    )
    out_specs = (P("pipe", "expert", None), P("pipe", "expert", None))
    return jax.shard_map(
        on_device, mesh=mesh, in_specs=in_specs, out_specs=out_specs, check_vma=False
    )
```

```python
import jax
import jax.numpy as jnp
from jax import lax
from jax.sharding import PartitionSpec as P


def shifted(block, axis, distance):
    devices = range(lax.axis_size(axis))
    route = [((i - distance) % len(devices), i) for i in devices]
    return lax.ppermute(block, axis, route)


def slot_table(routes, experts):
    route_hits = (routes[:, :, None] == jnp.arange(experts, dtype=jnp.int32)[None, None, :]).astype(
        jnp.int32
    )
    per_token = jnp.sum(route_hits, axis=1)
    before = jnp.cumsum(per_token, axis=0) - per_token
    return jnp.sum(route_hits * before[:, None, :], axis=2)


def slot_hits(routes, experts, capacity):
    slot_index = slot_table(routes, experts)
    flat_ids = routes * capacity + slot_index
    targets = jnp.arange(experts * capacity, dtype=jnp.int32)
    hits = (flat_ids[:, :, None] == targets[None, None, :]).astype(jnp.bfloat16)
    return hits.reshape(routes.shape[0], 2, experts, capacity)


def scaled_rows(cotangent, probs):
    return (probs[:, :, None] * cotangent[:, None, :].astype(jnp.float32)).astype(jnp.bfloat16)


def place(hits, rows):
    packed = lax.dot_general(
        hits, rows, (((0, 1), (0, 1)), ((), ())), preferred_element_type=jnp.float32
    )
    return packed.astype(jnp.bfloat16)


def place_tokens(tokens, hits):
    table = jnp.sum(hits, axis=1)
    packed = lax.dot_general(
        table, tokens, (((0,), (0,)), ((), ())), preferred_element_type=jnp.float32
    )
    return packed.astype(jnp.bfloat16)


def recompute(rows, gate_mat, up_mat):
    contract = (((2,), (0,)), ((), ()))
    gate_pre = lax.dot_general(rows, gate_mat, contract, preferred_element_type=jnp.float32)
    up_pre = lax.dot_general(rows, up_mat, contract, preferred_element_type=jnp.float32)
    return (gate_pre, up_pre)


def backprop(gate_pre, up_pre, scaled, gate_mat, up_mat, down_mat):
    contract = (((2,), (1,)), ((), ()))
    d_hidden = lax.dot_general(scaled, down_mat, contract, preferred_element_type=jnp.float32)
    gate_sig = jax.nn.sigmoid(gate_pre)
    active = gate_pre * gate_sig
    slope = gate_sig * (1.0 + gate_pre * (1.0 - gate_sig))
    d_gate = (d_hidden * up_pre * slope).astype(jnp.bfloat16)
    d_up = (d_hidden * active).astype(jnp.bfloat16)
    back = lax.dot_general(d_gate, gate_mat, contract, preferred_element_type=jnp.float32)
    back = back + lax.dot_general(d_up, up_mat, contract, preferred_element_type=jnp.float32)
    return back.astype(jnp.bfloat16)


def exchange(block):
    return lax.all_to_all(block, "expert", split_axis=0, concat_axis=0, tiled=True)


def pick(returned, hits, cotangent):
    table = jnp.sum(hits, axis=1)
    picked = lax.dot_general(
        table, returned, (((1, 2), (0, 1)), ((), ())), preferred_element_type=jnp.float32
    )
    summed = cotangent.astype(jnp.float32) + picked
    return summed.astype(jnp.bfloat16)


def back_half(d_gate, d_up, gate_mat, up_mat):
    contract = (((2,), (1,)), ((), ()))
    back = lax.dot_general(d_gate, gate_mat, contract, preferred_element_type=jnp.float32)
    back = back + lax.dot_general(d_up, up_mat, contract, preferred_element_type=jnp.float32)
    return back.astype(jnp.bfloat16)


def hidden_grads(gate_pre, up_pre, scaled, down_mat):
    contract = (((2,), (1,)), ((), ()))
    d_hidden = lax.dot_general(scaled, down_mat, contract, preferred_element_type=jnp.float32)
    gate_sig = jax.nn.sigmoid(gate_pre)
    active = gate_pre * gate_sig
    slope = gate_sig * (1.0 + gate_pre * (1.0 - gate_sig))
    d_gate = (d_hidden * up_pre * slope).astype(jnp.bfloat16)
    d_up = (d_hidden * active).astype(jnp.bfloat16)
    return d_gate, d_up


def pick_cols(returned, table):
    return lax.dot_general(
        table, returned, (((1, 2), (0, 1)), ((), ())), preferred_element_type=jnp.float32
    )


def beside(send, filler_input, filler, move=exchange):
    send, filler_input = lax.optimization_barrier((send, filler_input))
    arrived = move(send)
    extra = filler(filler_input)
    return lax.optimization_barrier((arrived, extra))


def on_device(
    tokens_a, cotangent_a, tokens_b, routes_a, routes_b, probs_a, probs_b, w_gate, w_up, w_down
):
    experts = lax.axis_size("expert")
    tok_count = tokens_a.shape[1]
    width = tokens_a.shape[2]
    capacity = 7 * tok_count // (2 * experts)
    gate_mat = w_gate[0, 0]
    up_mat = w_up[0, 0]
    down_mat = w_down[0, 0]
    contract = (((2,), (0,)), ((), ()))
    first_hits = slot_hits(routes_a[0], experts, capacity)
    first_cot = cotangent_a[0]

    first_rows = jnp.concatenate(
        [
            jnp.broadcast_to(tokens_a[0][:, None, :], (tok_count, 2, width)),
            scaled_rows(first_cot, probs_a[0]),
        ],
        axis=2,
    )

    def pack_second(pieces):
        routes, tokens = pieces
        hits = slot_hits(routes, experts, capacity)
        return hits, place_tokens(tokens, hits)

    first_arrived, (second_hits, second_send) = beside(
        place(first_hits, first_rows), (routes_b[0], tokens_b[0]), pack_second
    )

    def first_compute(arrived):
        gate_pre, up_pre = recompute(arrived[:, :, :width], gate_mat, up_mat)
        return backprop(gate_pre, up_pre, arrived[:, :, width:], gate_mat, up_mat, down_mat)

    second_tokens, first_back = beside(second_send, first_arrived, first_compute)
    returned, first_table = beside(first_back, first_hits, lambda hits: jnp.sum(hits, axis=1))
    picked = lax.dot_general(
        first_table, returned, (((1, 2), (0, 1)), ((), ())), preferred_element_type=jnp.float32
    )
    grad_a = (first_cot.astype(jnp.float32) + picked).astype(jnp.bfloat16)

    second_cot, second_gate_pre = beside(
        grad_a,
        second_tokens,
        lambda rows: lax.dot_general(rows, gate_mat, contract, preferred_element_type=jnp.float32),
        move=lambda block: shifted(block, "pipe", -1),
    )
    second_scaled, second_up_pre = beside(
        place(second_hits, scaled_rows(second_cot, probs_b[0])),
        second_tokens,
        lambda rows: lax.dot_general(rows, up_mat, contract, preferred_element_type=jnp.float32),
    )
    second_back = backprop(
        second_gate_pre, second_up_pre, second_scaled, gate_mat, up_mat, down_mat
    )
    second_returned, second_table = beside(
        second_back, second_hits, lambda hits: jnp.sum(hits, axis=1)
    )
    picked = lax.dot_general(
        second_table, second_returned, (((1, 2), (0, 1)), ((), ())),
        preferred_element_type=jnp.float32,
    )
    grad_b = (second_cot.astype(jnp.float32) + picked).astype(jnp.bfloat16)
    return (grad_a[None], grad_b[None])


def solution(mesh):
    in_specs = (
        P("pipe", "expert", None),
        P("pipe", "expert", None),
        P("pipe", "expert", None),
        P("pipe", "expert", None),
        P("pipe", "expert", None),
        P("pipe", "expert", None),
        P("pipe", "expert", None),
        P("pipe", "expert", None, None),
        P("pipe", "expert", None, None),
        P("pipe", "expert", None, None),
    )
    out_specs = (P("pipe", "expert", None), P("pipe", "expert", None))
    return jax.shard_map(
        on_device, mesh=mesh, in_specs=in_specs, out_specs=out_specs, check_vma=False
    )
```

```python
import jax
import jax.numpy as jnp
from jax import lax
from jax.sharding import PartitionSpec as P


def shifted(block, axis, distance):
    devices = range(lax.axis_size(axis))
    route = [((i - distance) % len(devices), i) for i in devices]
    return lax.ppermute(block, axis, route)


def slot_table(routes, experts):
    route_hits = (routes[:, :, None] == jnp.arange(experts, dtype=jnp.int32)[None, None, :]).astype(
        jnp.int32
    )
    per_token = jnp.sum(route_hits, axis=1)
    before = jnp.cumsum(per_token, axis=0) - per_token
    return jnp.sum(route_hits * before[:, None, :], axis=2)


def slot_hits(routes, experts, capacity):
    slot_index = slot_table(routes, experts)
    flat_ids = routes * capacity + slot_index
    targets = jnp.arange(experts * capacity, dtype=jnp.int32)
    hits = (flat_ids[:, :, None] == targets[None, None, :]).astype(jnp.bfloat16)
    return hits.reshape(routes.shape[0], 2, experts, capacity)


LANES = 128


def split_rows(x):
    return x.reshape(x.shape[:-1] + (x.shape[-1] // LANES, LANES))


def scaled_rows(cotangent, probs):
    return (probs[:, :, None] * cotangent[:, None, :].astype(jnp.float32)).astype(jnp.bfloat16)


def place(hits, rows):
    packed = lax.dot_general(
        hits, rows, (((0, 1), (0, 1)), ((), ())), preferred_element_type=jnp.float32
    )
    return packed.astype(jnp.bfloat16)


def place_tokens(tokens, hits):
    table = jnp.sum(hits, axis=1)
    packed = lax.dot_general(
        table, tokens, (((0,), (0,)), ((), ())), preferred_element_type=jnp.float32
    )
    return packed.astype(jnp.bfloat16)


def project(rows, mat):
    return lax.dot_general(
        rows, mat, (((2, 3), (0, 1)), ((), ())), preferred_element_type=jnp.float32
    )


def backprop(gate_pre, up_pre, scaled, gate_mat, up_mat, down_mat):
    d_hidden = lax.dot_general(
        scaled, down_mat, (((2, 3), (1, 2)), ((), ())), preferred_element_type=jnp.float32
    )
    gate_sig = jax.nn.sigmoid(gate_pre)
    active = gate_pre * gate_sig
    slope = gate_sig * (1.0 + gate_pre * (1.0 - gate_sig))
    d_gate = (d_hidden * up_pre * slope).astype(jnp.bfloat16)
    d_up = (d_hidden * active).astype(jnp.bfloat16)
    contract = (((2,), (2,)), ((), ()))
    back = lax.dot_general(d_gate, gate_mat, contract, preferred_element_type=jnp.float32)
    back = back + lax.dot_general(d_up, up_mat, contract, preferred_element_type=jnp.float32)
    return back.astype(jnp.bfloat16)


def exchange(block):
    return lax.all_to_all(block, "expert", split_axis=0, concat_axis=0, tiled=True)


def beside(send, filler_input, filler, move=exchange):
    send, filler_input = lax.optimization_barrier((send, filler_input))
    arrived = move(send)
    extra = filler(filler_input)
    return lax.optimization_barrier((arrived, extra))


def combine(cotangent, table, returned):
    picked = lax.dot_general(
        table, returned, (((1, 2), (0, 1)), ((), ())), preferred_element_type=jnp.float32
    )
    summed = split_rows(cotangent).astype(jnp.float32) + picked
    return summed.astype(jnp.bfloat16).reshape(cotangent.shape)


def on_device(
    tokens_a, cotangent_a, tokens_b, routes_a, routes_b, probs_a, probs_b, w_gate, w_up, w_down
):
    experts = lax.axis_size("expert")
    tok_count = tokens_a.shape[1]
    width = tokens_a.shape[2]
    lanes_k = width // LANES
    capacity = 7 * tok_count // (2 * experts)
    gate_mat = w_gate[0, 0].reshape(lanes_k, LANES, -1)
    up_mat = w_up[0, 0].reshape(lanes_k, LANES, -1)
    first_hits = slot_hits(routes_a[0], experts, capacity)
    first_cot = cotangent_a[0]

    first_rows = split_rows(
        jnp.concatenate(
            [
                jnp.broadcast_to(tokens_a[0][:, None, :], (tok_count, 2, width)),
                scaled_rows(first_cot, probs_a[0]),
            ],
            axis=2,
        )
    )

    def pack_second(pieces):
        routes, tokens, down = pieces
        hits = slot_hits(routes, experts, capacity)
        return hits, place_tokens(split_rows(tokens), hits), split_rows(down)

    first_arrived, (second_hits, second_send, down_mat) = beside(
        place(first_hits, first_rows), (routes_b[0], tokens_b[0], w_down[0, 0]), pack_second
    )

    def first_compute(arrived):
        gate_pre = project(arrived[:, :, :lanes_k], gate_mat)
        up_pre = project(arrived[:, :, :lanes_k], up_mat)
        return backprop(
            gate_pre, up_pre, arrived[:, :, lanes_k:], gate_mat, up_mat, down_mat
        )

    second_tokens, first_back = beside(second_send, first_arrived, first_compute)
    returned, first_table = beside(first_back, first_hits, lambda hits: jnp.sum(hits, axis=1))
    grad_a = combine(first_cot, first_table, returned)

    second_cot, second_gate_pre = beside(
        grad_a,
        second_tokens,
        lambda rows: project(rows, gate_mat),
        move=lambda block: shifted(block, "pipe", -1),
    )
    second_scaled, second_up_pre = beside(
        place(second_hits, split_rows(scaled_rows(second_cot, probs_b[0]))),
        second_tokens,
        lambda rows: project(rows, up_mat),
    )
    second_back = backprop(
        second_gate_pre, second_up_pre, second_scaled, gate_mat, up_mat, down_mat
    )
    second_returned, second_table = beside(
        second_back, second_hits, lambda hits: jnp.sum(hits, axis=1)
    )
    grad_b = combine(second_cot, second_table, second_returned)
    return (grad_a[None], grad_b[None])


def solution(mesh):
    in_specs = (
        P("pipe", "expert", None),
        P("pipe", "expert", None),
        P("pipe", "expert", None),
        P("pipe", "expert", None),
        P("pipe", "expert", None),
        P("pipe", "expert", None),
        P("pipe", "expert", None),
        P("pipe", "expert", None, None),
        P("pipe", "expert", None, None),
        P("pipe", "expert", None, None),
    )
    out_specs = (P("pipe", "expert", None), P("pipe", "expert", None))
    return jax.shard_map(
        on_device, mesh=mesh, in_specs=in_specs, out_specs=out_specs, check_vma=False
    )
```

```python
import jax
import jax.numpy as jnp
from jax import lax
from jax.sharding import PartitionSpec as P


def shifted(block, axis, distance):
    devices = range(lax.axis_size(axis))
    route = [((i - distance) % len(devices), i) for i in devices]
    return lax.ppermute(block, axis, route)


def slot_table(routes, experts):
    route_hits = (routes[:, :, None] == jnp.arange(experts, dtype=jnp.int32)[None, None, :]).astype(
        jnp.int32
    )
    per_token = jnp.sum(route_hits, axis=1)
    before = jnp.cumsum(per_token, axis=0) - per_token
    return jnp.sum(route_hits * before[:, None, :], axis=2)


def slot_hits(routes, experts, capacity):
    slot_index = slot_table(routes, experts)
    flat_ids = routes * capacity + slot_index
    targets = jnp.arange(experts * capacity, dtype=jnp.int32)
    hits = (flat_ids[:, :, None] == targets[None, None, :]).astype(jnp.bfloat16)
    return hits.reshape(routes.shape[0], 2, experts, capacity)


LANES = 128


def split_rows(x):
    return x.reshape(x.shape[:-1] + (x.shape[-1] // LANES, LANES))


def scaled_rows(cotangent, probs):
    scaled = probs[:, :, None, None] * cotangent[:, None].astype(jnp.float32)
    return scaled.astype(jnp.bfloat16)


def place(hits, rows):
    packed = lax.dot_general(
        hits, rows, (((0, 1), (0, 1)), ((), ())), preferred_element_type=jnp.float32
    )
    return packed.astype(jnp.bfloat16)


def place_tokens(tokens, hits):
    table = jnp.sum(hits, axis=1)
    packed = lax.dot_general(
        table, tokens, (((0,), (0,)), ((), ())), preferred_element_type=jnp.float32
    )
    return packed.astype(jnp.bfloat16)


def project(rows, mat):
    return lax.dot_general(
        rows, mat, (((2, 3), (0, 1)), ((), ())), preferred_element_type=jnp.float32
    )


def backprop(gate_pre, up_pre, scaled, gate_mat, up_mat, down_mat):
    d_hidden = lax.dot_general(
        scaled, down_mat, (((2, 3), (1, 2)), ((), ())), preferred_element_type=jnp.float32
    )
    gate_sig = jax.nn.sigmoid(gate_pre)
    active = gate_pre * gate_sig
    slope = gate_sig * (1.0 + gate_pre * (1.0 - gate_sig))
    d_gate = (d_hidden * up_pre * slope).astype(jnp.bfloat16)
    d_up = (d_hidden * active).astype(jnp.bfloat16)
    contract = (((2,), (2,)), ((), ()))
    back = lax.dot_general(d_gate, gate_mat, contract, preferred_element_type=jnp.float32)
    back = back + lax.dot_general(d_up, up_mat, contract, preferred_element_type=jnp.float32)
    return back.astype(jnp.bfloat16)


def exchange(block):
    return lax.all_to_all(block, "expert", split_axis=0, concat_axis=0, tiled=True)


def beside(send, filler_input, filler, move=exchange):
    send, filler_input = lax.optimization_barrier((send, filler_input))
    arrived = move(send)
    extra = filler(filler_input)
    return lax.optimization_barrier((arrived, extra))


def combine(cotangent, table, returned):
    picked = lax.dot_general(
        table, returned, (((1, 2), (0, 1)), ((), ())), preferred_element_type=jnp.float32
    )
    summed = cotangent.astype(jnp.float32) + picked
    return summed.astype(jnp.bfloat16)


def on_device(
    tokens_a, cotangent_a, tokens_b, routes_a, routes_b, probs_a, probs_b, w_gate, w_up, w_down
):
    experts = lax.axis_size("expert")
    tok_count = tokens_a.shape[1]
    width = tokens_a.shape[2]
    lanes_k = width // LANES
    capacity = 7 * tok_count // (2 * experts)
    gate_mat = w_gate[0, 0].reshape(lanes_k, LANES, -1)
    up_mat = w_up[0, 0].reshape(lanes_k, LANES, -1)
    first_hits = slot_hits(routes_a[0], experts, capacity)
    first_cot, first_tok = lax.optimization_barrier(
        (split_rows(cotangent_a[0]), split_rows(tokens_a[0]))
    )

    first_rows = jnp.concatenate(
        [
            jnp.broadcast_to(first_tok[:, None], (tok_count, 2, lanes_k, LANES)),
            scaled_rows(first_cot, probs_a[0]),
        ],
        axis=2,
    )

    def pack_second(pieces):
        routes, tokens, down = pieces
        hits = slot_hits(routes, experts, capacity)
        return hits, place_tokens(split_rows(tokens), hits), split_rows(down)

    first_arrived, (second_hits, second_send, down_mat) = beside(
        place(first_hits, first_rows), (routes_b[0], tokens_b[0], w_down[0, 0]), pack_second
    )

    def first_compute(arrived):
        gate_pre = project(arrived[:, :, :lanes_k], gate_mat)
        up_pre = project(arrived[:, :, :lanes_k], up_mat)
        return backprop(
            gate_pre, up_pre, arrived[:, :, lanes_k:], gate_mat, up_mat, down_mat
        )

    second_tokens, first_back = beside(second_send, first_arrived, first_compute)
    returned, first_table = beside(first_back, first_hits, lambda hits: jnp.sum(hits, axis=1))
    grad_a = combine(first_cot, first_table, returned)

    second_cot, (second_gate_pre, second_up_pre) = beside(
        grad_a,
        second_tokens,
        lambda rows: (project(rows, gate_mat), project(rows, up_mat)),
        move=lambda block: shifted(block, "pipe", -1),
    )
    second_scaled, second_table = beside(
        place(second_hits, scaled_rows(second_cot, probs_b[0])),
        second_hits,
        lambda hits: jnp.sum(hits, axis=1),
    )
    second_back = backprop(
        second_gate_pre, second_up_pre, second_scaled, gate_mat, up_mat, down_mat
    )
    second_returned, grad_a = beside(
        second_back, grad_a, lambda rows: rows.reshape(tok_count, width)
    )
    grad_b = combine(second_cot, second_table, second_returned).reshape(tok_count, width)
    return (grad_a[None], grad_b[None])


def solution(mesh):
    in_specs = (
        P("pipe", "expert", None),
        P("pipe", "expert", None),
        P("pipe", "expert", None),
        P("pipe", "expert", None),
        P("pipe", "expert", None),
        P("pipe", "expert", None),
        P("pipe", "expert", None),
        P("pipe", "expert", None, None),
        P("pipe", "expert", None, None),
        P("pipe", "expert", None, None),
    )
    out_specs = (P("pipe", "expert", None), P("pipe", "expert", None))
    return jax.shard_map(
        on_device, mesh=mesh, in_specs=in_specs, out_specs=out_specs, check_vma=False
    )
```

```python
import jax
import jax.numpy as jnp
from jax import lax
from jax.sharding import PartitionSpec as P
from jax.experimental.layout import Layout, with_layout_constraint


def shifted(block, axis, distance):
    devices = range(lax.axis_size(axis))
    route = [((i - distance) % len(devices), i) for i in devices]
    return lax.ppermute(block, axis, route)


def slot_table(routes, experts):
    route_hits = (routes[:, :, None] == jnp.arange(experts, dtype=jnp.int32)[None, None, :]).astype(
        jnp.int32
    )
    per_token = jnp.sum(route_hits, axis=1)
    before = jnp.cumsum(per_token, axis=0) - per_token
    return jnp.sum(route_hits * before[:, None, :], axis=2)


def slot_hits(routes, experts, capacity):
    slot_index = slot_table(routes, experts)
    flat_ids = routes * capacity + slot_index
    targets = jnp.arange(experts * capacity, dtype=jnp.int32)
    hits = (flat_ids[:, :, None] == targets[None, None, :]).astype(jnp.bfloat16)
    return hits.reshape(routes.shape[0], 2, experts, capacity)


LANES = 128


def split_rows(x):
    return x.reshape(x.shape[:-1] + (x.shape[-1] // LANES, LANES))


def scaled_rows(cotangent, probs):
    scaled = probs[:, :, None, None] * cotangent[:, None].astype(jnp.float32)
    return scaled.astype(jnp.bfloat16)


def place(hits, rows):
    packed = lax.dot_general(
        hits, rows, (((0, 1), (0, 1)), ((), ())), preferred_element_type=jnp.float32
    )
    return packed.astype(jnp.bfloat16)


def place_tokens(tokens, hits):
    table = jnp.sum(hits, axis=1)
    packed = lax.dot_general(
        table, tokens, (((0,), (0,)), ((), ())), preferred_element_type=jnp.float32
    )
    return with_layout_constraint(packed.astype(jnp.bfloat16), Layout((0, 1, 2, 3)))


def project(rows, mat):
    return lax.dot_general(
        rows, mat, (((2, 3), (0, 1)), ((), ())), preferred_element_type=jnp.float32
    )


def backprop(gate_pre, up_pre, scaled, gate_mat, up_mat, down_mat):
    d_hidden = lax.dot_general(
        scaled, down_mat, (((2, 3), (1, 2)), ((), ())), preferred_element_type=jnp.float32
    )
    gate_sig = jax.nn.sigmoid(gate_pre)
    active = gate_pre * gate_sig
    slope = gate_sig * (1.0 + gate_pre * (1.0 - gate_sig))
    d_gate = (d_hidden * up_pre * slope).astype(jnp.bfloat16)
    d_up = (d_hidden * active).astype(jnp.bfloat16)
    contract = (((2,), (2,)), ((), ()))
    back = lax.dot_general(d_gate, gate_mat, contract, preferred_element_type=jnp.float32)
    back = back + lax.dot_general(d_up, up_mat, contract, preferred_element_type=jnp.float32)
    return back.astype(jnp.bfloat16)


def exchange(block):
    return lax.all_to_all(block, "expert", split_axis=0, concat_axis=0, tiled=True)


def beside(send, filler_input, filler, move=exchange):
    send, filler_input = lax.optimization_barrier((send, filler_input))
    arrived = move(send)
    extra = filler(filler_input)
    return lax.optimization_barrier((arrived, extra))


def combine(cotangent, table, returned):
    picked = lax.dot_general(
        table, returned, (((1, 2), (0, 1)), ((), ())), preferred_element_type=jnp.float32
    )
    summed = cotangent.astype(jnp.float32) + picked
    return summed.astype(jnp.bfloat16)


def on_device(
    tokens_a, cotangent_a, tokens_b, routes_a, routes_b, probs_a, probs_b, w_gate, w_up, w_down
):
    experts = lax.axis_size("expert")
    tok_count = tokens_a.shape[1]
    width = tokens_a.shape[2]
    lanes_k = width // LANES
    capacity = 7 * tok_count // (2 * experts)
    gate_mat = w_gate[0, 0].reshape(lanes_k, LANES, -1)
    up_mat = w_up[0, 0].reshape(lanes_k, LANES, -1)
    first_hits = slot_hits(routes_a[0], experts, capacity)
    first_cot, first_tok = lax.optimization_barrier(
        (split_rows(cotangent_a[0]), split_rows(tokens_a[0]))
    )

    first_rows = jnp.concatenate(
        [
            jnp.broadcast_to(first_tok[:, None], (tok_count, 2, lanes_k, LANES)),
            scaled_rows(first_cot, probs_a[0]),
        ],
        axis=2,
    )

    def pack_second(pieces):
        routes, tokens, down = pieces
        hits = slot_hits(routes, experts, capacity)
        return hits, place_tokens(split_rows(tokens), hits), split_rows(down)

    first_arrived, (second_hits, second_send, down_mat) = beside(
        place(first_hits, first_rows), (routes_b[0], tokens_b[0], w_down[0, 0]), pack_second
    )

    def first_compute(arrived):
        gate_pre = project(arrived[:, :, :lanes_k], gate_mat)
        up_pre = project(arrived[:, :, :lanes_k], up_mat)
        return backprop(
            gate_pre, up_pre, arrived[:, :, lanes_k:], gate_mat, up_mat, down_mat
        )

    second_tokens, first_back = beside(second_send, first_arrived, first_compute)
    returned, first_table = beside(first_back, first_hits, lambda hits: jnp.sum(hits, axis=1))
    grad_a = combine(first_cot, first_table, returned)

    second_cot, (second_gate_pre, second_up_pre) = beside(
        grad_a,
        second_tokens,
        lambda rows: (project(rows, gate_mat), project(rows, up_mat)),
        move=lambda block: shifted(block, "pipe", -1),
    )
    second_scaled, second_table = beside(
        place(second_hits, scaled_rows(second_cot, probs_b[0])),
        second_hits,
        lambda hits: jnp.sum(hits, axis=1),
    )
    second_back = backprop(
        second_gate_pre, second_up_pre, second_scaled, gate_mat, up_mat, down_mat
    )
    second_returned, grad_a = beside(
        second_back, grad_a, lambda rows: rows.reshape(tok_count, width)
    )
    grad_b = combine(second_cot, second_table, second_returned).reshape(tok_count, width)
    return (grad_a[None], grad_b[None])


def solution(mesh):
    in_specs = (
        P("pipe", "expert", None),
        P("pipe", "expert", None),
        P("pipe", "expert", None),
        P("pipe", "expert", None),
        P("pipe", "expert", None),
        P("pipe", "expert", None),
        P("pipe", "expert", None),
        P("pipe", "expert", None, None),
        P("pipe", "expert", None, None),
        P("pipe", "expert", None, None),
    )
    out_specs = (P("pipe", "expert", None), P("pipe", "expert", None))
    return jax.shard_map(
        on_device, mesh=mesh, in_specs=in_specs, out_specs=out_specs, check_vma=False
    )
```

```python
import jax
import jax.numpy as jnp
from jax import lax
from jax.sharding import PartitionSpec as P
from jax.experimental.layout import Layout, with_layout_constraint


def shifted(block, axis, distance):
    devices = range(lax.axis_size(axis))
    route = [((i - distance) % len(devices), i) for i in devices]
    return lax.ppermute(block, axis, route)


def slot_table(routes, experts):
    route_hits = (routes[:, :, None] == jnp.arange(experts, dtype=jnp.int32)[None, None, :]).astype(
        jnp.int32
    )
    per_token = jnp.sum(route_hits, axis=1)
    before = jnp.cumsum(per_token, axis=0) - per_token
    return jnp.sum(route_hits * before[:, None, :], axis=2)


def slot_hits(routes, experts, capacity):
    slot_index = slot_table(routes, experts)
    flat_ids = routes * capacity + slot_index
    targets = jnp.arange(experts * capacity, dtype=jnp.int32)
    hits = (flat_ids[:, :, None] == targets[None, None, :]).astype(jnp.bfloat16)
    return hits.reshape(routes.shape[0], 2, experts, capacity)


LANES = 128


def split_rows(x):
    return x.reshape(x.shape[:-1] + (x.shape[-1] // LANES, LANES))


def scaled_rows(cotangent, probs):
    scaled = probs[:, :, None, None] * cotangent[:, None].astype(jnp.float32)
    return scaled.astype(jnp.bfloat16)


def place(hits, rows):
    packed = lax.dot_general(
        hits, rows, (((0, 1), (0, 1)), ((), ())), preferred_element_type=jnp.float32
    )
    return packed.astype(jnp.bfloat16)


def place_tokens(tokens, hits):
    table = jnp.sum(hits, axis=1)
    packed = lax.dot_general(
        table, tokens, (((0,), (0,)), ((), ())), preferred_element_type=jnp.float32
    )
    return with_layout_constraint(packed.astype(jnp.bfloat16), Layout((0, 1, 2, 3)))


def project(rows, mat):
    return lax.dot_general(
        rows, mat, (((2, 3), (0, 1)), ((), ())), preferred_element_type=jnp.float32
    )


def backprop(gate_pre, up_pre, scaled, gate_mat, up_mat, down_mat):
    d_hidden = lax.dot_general(
        scaled, down_mat, (((2, 3), (1, 2)), ((), ())), preferred_element_type=jnp.float32
    )
    gate_sig = jax.nn.sigmoid(gate_pre)
    active = gate_pre * gate_sig
    slope = gate_sig * (1.0 + gate_pre * (1.0 - gate_sig))
    d_gate = (d_hidden * up_pre * slope).astype(jnp.bfloat16)
    d_up = (d_hidden * active).astype(jnp.bfloat16)
    contract = (((2,), (2,)), ((), ()))
    back = lax.dot_general(d_gate, gate_mat, contract, preferred_element_type=jnp.float32)
    back = back + lax.dot_general(d_up, up_mat, contract, preferred_element_type=jnp.float32)
    return back.astype(jnp.bfloat16)


def exchange(block):
    return lax.all_to_all(block, "expert", split_axis=0, concat_axis=0, tiled=True)


def beside(send, filler_input, filler, move=exchange):
    send, filler_input = lax.optimization_barrier((send, filler_input))
    arrived = move(send)
    extra = filler(filler_input)
    return lax.optimization_barrier((arrived, extra))


def combine(cotangent, table, returned):
    picked = lax.dot_general(
        table, returned, (((1, 2), (0, 1)), ((), ())), preferred_element_type=jnp.float32
    )
    summed = cotangent.astype(jnp.float32) + picked
    return summed.astype(jnp.bfloat16)


def on_device(
    tokens_a, cotangent_a, tokens_b, routes_a, routes_b, probs_a, probs_b, w_gate, w_up, w_down
):
    experts = lax.axis_size("expert")
    tok_count = tokens_a.shape[1]
    width = tokens_a.shape[2]
    lanes_k = width // LANES
    capacity = 7 * tok_count // (2 * experts)
    gate_mat = w_gate[0, 0].reshape(lanes_k, LANES, -1)
    up_mat = w_up[0, 0].reshape(lanes_k, LANES, -1)
    first_hits = slot_hits(routes_a[0], experts, capacity)
    first_cot, first_tok = lax.optimization_barrier(
        (split_rows(cotangent_a[0]), split_rows(tokens_a[0]))
    )

    first_rows = jnp.concatenate(
        [
            jnp.broadcast_to(first_tok[:, None], (tok_count, 2, lanes_k, LANES)),
            scaled_rows(first_cot, probs_a[0]),
        ],
        axis=2,
    )

    def pack_second(pieces):
        routes, tokens, down = pieces
        hits = slot_hits(routes, experts, capacity)
        return hits, place_tokens(split_rows(tokens), hits), split_rows(down)

    first_arrived, (second_hits, second_send, down_mat) = beside(
        place(first_hits, first_rows), (routes_b[0], tokens_b[0], w_down[0, 0]), pack_second
    )

    def first_compute(arrived):
        gate_pre = project(arrived[:, :, :lanes_k], gate_mat)
        up_pre = project(arrived[:, :, :lanes_k], up_mat)
        return backprop(
            gate_pre, up_pre, arrived[:, :, lanes_k:], gate_mat, up_mat, down_mat
        )

    second_tokens, first_back = beside(second_send, first_arrived, first_compute)
    returned, first_table = beside(first_back, first_hits, lambda hits: jnp.sum(hits, axis=1))
    grad_a = combine(first_cot, first_table, returned)

    second_cot, (second_gate_pre, second_up_pre) = beside(
        grad_a,
        second_tokens,
        lambda rows: (project(rows, gate_mat), project(rows, up_mat)),
        move=lambda block: shifted(block, "pipe", -1),
    )
    second_scaled, second_table = beside(
        place(second_hits, scaled_rows(second_cot, probs_b[0])),
        second_hits,
        lambda hits: jnp.sum(hits, axis=1),
    )
    second_back = backprop(
        second_gate_pre, second_up_pre, second_scaled, gate_mat, up_mat, down_mat
    )
    second_returned, grad_a = beside(
        second_back,
        grad_a,
        lambda rows: with_layout_constraint(rows.reshape(1, tok_count, width), Layout((0, 1, 2))),
    )
    grad_b = combine(second_cot, second_table, second_returned).reshape(1, tok_count, width)
    return (grad_a, with_layout_constraint(grad_b, Layout((0, 1, 2))))


def solution(mesh):
    in_specs = (
        P("pipe", "expert", None),
        P("pipe", "expert", None),
        P("pipe", "expert", None),
        P("pipe", "expert", None),
        P("pipe", "expert", None),
        P("pipe", "expert", None),
        P("pipe", "expert", None),
        P("pipe", "expert", None, None),
        P("pipe", "expert", None, None),
        P("pipe", "expert", None, None),
    )
    out_specs = (P("pipe", "expert", None), P("pipe", "expert", None))
    return jax.shard_map(
        on_device, mesh=mesh, in_specs=in_specs, out_specs=out_specs, check_vma=False
    )
```

```python
import jax
import jax.numpy as jnp
from jax import lax
from jax.sharding import PartitionSpec as P
from jax.experimental.layout import Layout, with_layout_constraint


def shifted(block, axis, distance):
    devices = range(lax.axis_size(axis))
    route = [((i - distance) % len(devices), i) for i in devices]
    return lax.ppermute(block, axis, route)


def slot_table(routes, experts):
    route_hits = (routes[:, :, None] == jnp.arange(experts, dtype=jnp.int32)[None, None, :]).astype(
        jnp.int32
    )
    per_token = jnp.sum(route_hits, axis=1)
    before = jnp.cumsum(per_token, axis=0) - per_token
    return jnp.sum(route_hits * before[:, None, :], axis=2)


def slot_hits(routes, experts, capacity):
    slot_index = slot_table(routes, experts)
    flat_ids = routes * capacity + slot_index
    targets = jnp.arange(experts * capacity, dtype=jnp.int32)
    hits = (flat_ids[:, :, None] == targets[None, None, :]).astype(jnp.bfloat16)
    return hits.reshape(routes.shape[0], 2, experts, capacity)


LANES = 128


def split_rows(x):
    return x.reshape(x.shape[:-1] + (x.shape[-1] // LANES, LANES))


def scaled_rows(cotangent, probs):
    scaled = probs[:, :, None, None] * cotangent[:, None].astype(jnp.float32)
    return scaled.astype(jnp.bfloat16)


def place(hits, rows):
    packed = lax.dot_general(
        hits, rows, (((0, 1), (0, 1)), ((), ())), preferred_element_type=jnp.float32
    )
    return packed.astype(jnp.bfloat16)


def place_tokens(tokens, hits):
    table = jnp.sum(hits, axis=1)
    packed = lax.dot_general(
        table, tokens, (((0,), (0,)), ((), ())), preferred_element_type=jnp.float32
    )
    return with_layout_constraint(packed.astype(jnp.bfloat16), Layout((0, 1, 2, 3)))


def project(rows, mat):
    return lax.dot_general(
        rows, mat, (((2, 3), (0, 1)), ((), ())), preferred_element_type=jnp.float32
    )


def backprop(gate_pre, up_pre, scaled, gate_mat, up_mat, down_mat):
    d_hidden = lax.dot_general(
        scaled, down_mat, (((2, 3), (1, 2)), ((), ())), preferred_element_type=jnp.float32
    )
    gate_sig = jax.nn.sigmoid(gate_pre)
    active = gate_pre * gate_sig
    slope = gate_sig * (1.0 + gate_pre * (1.0 - gate_sig))
    d_gate = (d_hidden * up_pre * slope).astype(jnp.bfloat16)
    d_up = (d_hidden * active).astype(jnp.bfloat16)
    contract = (((2,), (2,)), ((), ()))
    back = lax.dot_general(d_gate, gate_mat, contract, preferred_element_type=jnp.float32)
    back = back + lax.dot_general(d_up, up_mat, contract, preferred_element_type=jnp.float32)
    return back.astype(jnp.bfloat16)


def exchange(block):
    return lax.all_to_all(block, "expert", split_axis=0, concat_axis=0, tiled=True)


def beside(send, filler_input, filler, move=exchange):
    send, filler_input = lax.optimization_barrier((send, filler_input))
    arrived = move(send)
    extra = filler(filler_input)
    return lax.optimization_barrier((arrived, extra))


def combine(cotangent, table, returned):
    picked = lax.dot_general(
        table, returned, (((1, 2), (0, 1)), ((), ())), preferred_element_type=jnp.float32
    )
    summed = cotangent.astype(jnp.float32) + picked
    return summed.astype(jnp.bfloat16)


def on_device(
    tokens_a, cotangent_a, tokens_b, routes_a, routes_b, probs_a, probs_b, w_gate, w_up, w_down
):
    experts = lax.axis_size("expert")
    tok_count = tokens_a.shape[1]
    width = tokens_a.shape[2]
    lanes_k = width // LANES
    capacity = 7 * tok_count // (2 * experts)
    gate_mat = w_gate[0, 0].reshape(lanes_k, LANES, -1)
    up_mat = w_up[0, 0].reshape(lanes_k, LANES, -1)
    first_hits = slot_hits(routes_a[0], experts, capacity)
    first_cot, first_tok = lax.optimization_barrier(
        (split_rows(cotangent_a[0]), split_rows(tokens_a[0]))
    )

    first_rows = jnp.concatenate(
        [
            jnp.broadcast_to(first_tok[:, None], (tok_count, 2, lanes_k, LANES)),
            scaled_rows(first_cot, probs_a[0]),
        ],
        axis=2,
    )

    def pack_second(pieces):
        routes, tokens, down = pieces
        hits = slot_hits(routes, experts, capacity)
        return hits, place_tokens(split_rows(tokens), hits), split_rows(down)

    first_arrived, (second_hits, second_send, down_mat) = beside(
        place(first_hits, first_rows), (routes_b[0], tokens_b[0], w_down[0, 0]), pack_second
    )

    def first_compute(arrived):
        gate_pre = project(arrived[:, :, :lanes_k], gate_mat)
        up_pre = project(arrived[:, :, :lanes_k], up_mat)
        return backprop(
            gate_pre, up_pre, arrived[:, :, lanes_k:], gate_mat, up_mat, down_mat
        )

    second_tokens, first_back = beside(second_send, first_arrived, first_compute)
    returned, first_table = beside(first_back, first_hits, lambda hits: jnp.sum(hits, axis=1))
    grad_a = combine(first_cot, first_table, returned)

    second_cot, (second_gate_pre, second_up_pre) = beside(
        grad_a,
        second_tokens,
        lambda rows: (project(rows, gate_mat), project(rows, up_mat)),
        move=lambda block: shifted(block, "pipe", -1),
    )
    second_scaled, second_table = beside(
        place(second_hits, scaled_rows(second_cot, probs_b[0])),
        second_hits,
        lambda hits: jnp.sum(hits, axis=1),
    )
    second_back = backprop(
        second_gate_pre, second_up_pre, second_scaled, gate_mat, up_mat, down_mat
    )
    second_returned, grad_a = beside(
        second_back,
        grad_a,
        lambda rows: with_layout_constraint(rows.reshape(1, tok_count, width), Layout((0, 1, 2))),
    )
    grad_b = with_layout_constraint(
        combine(second_cot, second_table, second_returned), Layout((0, 1, 2))
    ).reshape(1, tok_count, width)
    return (grad_a, with_layout_constraint(grad_b, Layout((0, 1, 2))))


def solution(mesh):
    in_specs = (
        P("pipe", "expert", None),
        P("pipe", "expert", None),
        P("pipe", "expert", None),
        P("pipe", "expert", None),
        P("pipe", "expert", None),
        P("pipe", "expert", None),
        P("pipe", "expert", None),
        P("pipe", "expert", None, None),
        P("pipe", "expert", None, None),
        P("pipe", "expert", None, None),
    )
    out_specs = (P("pipe", "expert", None), P("pipe", "expert", None))
    return jax.shard_map(
        on_device, mesh=mesh, in_specs=in_specs, out_specs=out_specs, check_vma=False
    )
```
